768 devices in a mesh: section: 12 (over z), tensor: 64 (over x, y, core).
Axes of the slice: x: 4, y: 8, z: 12, core: 2. Of those that a mesh axis runs over, the one named last changes fastest.
Arguments:
- hidden: bfloat16 [192, 8192], P('section'), may hold values from -600 to 600
- norm_gain: bfloat16 [8192], replicated, may hold values from 0.5 to 1.5
- targets: int32 [192], replicated, may hold values from 0 to 98303
- out_weight: bfloat16 [8192, 98304], P(None, ('section', 'tensor')), may hold values from -1 to 1
Outputs:
- token_loss: float32 [192], replicated
- grad_normed: bfloat16 [192, 8192], P('section', 'tensor')
- grad_weight: bfloat16 [8192, 98304], P(None, ('section', 'tensor'))
- normed_rows: bfloat16 [192, 8192], P('section', 'tensor')
The draws below stay inside these ranges and needn't reach their ends.
All inputs are finite; a program needn't handle non-finite values.
Results may differ from the reference program's by a relative error of at most 0.0073.
Values may be sent and summed in bfloat16 or wider, within the bound.
No kernel may reach another device: no remote copies, remote signals or barrier semaphores. Data moves between devices by JAX's collectives and lax.ppermute only.
A program may use at most 32 MiB of HBM per device.

```python
import math
import jax
import jax.numpy as jnp
from jax import lax

D = 8192
VOCAB = 98304
TOK = 192


def feature_scales(key):
    return jnp.exp(jax.random.uniform(jax.random.fold_in(key, 11), (D,), jnp.float32, 0.0, math.log(10.0)))


def draw_hidden(key, part):
    feature_scale = feature_scales(key)
    row_scale = jnp.exp(jax.random.uniform(jax.random.fold_in(key, 2), (TOK, 1), jnp.float32, 0.0, math.log(10.0)))
    noise_values = jnp.clip(jax.random.normal(jax.random.fold_in(key, 3), (TOK, D), jnp.float32), -6.0, 6.0)
    values = noise_values * row_scale * feature_scale[None, :]
    return values.astype(jnp.bfloat16)


def draw_out_weight(key, part):
    weight_scale = 1.5 / math.sqrt(D)
    values = jnp.clip(jax.random.normal(jax.random.fold_in(key, 5), (D, VOCAB), jnp.float32), -6.0, 6.0) * weight_scale
    return values.astype(jnp.bfloat16)


def place_ends(drawn, own_key, low, top_value):
    spot = [jax.random.randint(jax.random.fold_in(own_key, axis), (), 0, length) for axis, length in enumerate(drawn.shape)]
    main_axis = drawn.shape.index(max(drawn.shape))
    beside = spot[:main_axis] + [(spot[main_axis] + 1) % drawn.shape[main_axis]] + spot[main_axis + 1:]
    return drawn.at[tuple(spot)].set(low).at[tuple(beside)].set(top_value)


def setup_inputs(seed: int = 0) -> dict:
    key_list = jax.random.split(jax.random.key(seed), 5)
    hidden = draw_hidden(jax.random.fold_in(key_list[4], 71), 0)
    norm_gain = jnp.clip(1.0 + 0.1 * jax.random.normal(key_list[1], (D,), jnp.float32), 0.5, 1.5).astype(jnp.bfloat16)
    targets = place_ends(jax.random.randint(key_list[2], (TOK,), 0, VOCAB), jax.random.fold_in(key_list[2], 1), 0, VOCAB - 1).astype(jnp.int32)
    out_weight = draw_out_weight(jax.random.fold_in(key_list[4], 71), 0)
    return {"hidden": hidden, "norm_gain": norm_gain, "targets": targets, "out_weight": out_weight}


def reference(hidden, norm_gain, targets, out_weight):
    row_values = hidden.astype(jnp.float32)
    inv_rms = lax.rsqrt(lax.optimization_barrier(jnp.mean(row_values * row_values, axis=-1, keepdims=True)) + 1e-05)
    normed = (row_values * inv_rms * norm_gain.astype(jnp.float32)[None, :]).astype(jnp.bfloat16)
    logits = jnp.dot(normed, out_weight, preferred_element_type=jnp.float32)
    row_peak = lax.optimization_barrier(jnp.max(logits, axis=1))
    weights = jnp.exp(logits - row_peak[:, None])
    row_total = lax.optimization_barrier(jnp.sum(weights, axis=1))
    vocab_ids = jnp.arange(VOCAB, dtype=jnp.int32)
    target_hits = (targets[:, None] == vocab_ids[None, :]).astype(jnp.float32)
    target_logit = lax.optimization_barrier(jnp.sum(logits * target_hits, axis=1))
    token_loss = row_peak + jnp.log(row_total) - target_logit
    shares = weights / row_total[:, None]
    probs = shares.astype(jnp.bfloat16)
    grad_logits = (shares - target_hits).astype(jnp.bfloat16)
    grad_weight = lax.dot_general(normed, probs, (((0,), (0,)), ((), ())), preferred_element_type=jnp.float32).astype(jnp.bfloat16)
    grad_normed = lax.dot_general(grad_logits, out_weight, (((1,), (1,)), ((), ())), preferred_element_type=jnp.float32).astype(jnp.bfloat16)
    return (token_loss, grad_normed, grad_weight, normed)
```

```python
import jax
import jax.numpy as jnp
from jax import lax
from jax.sharding import PartitionSpec as P

ALL = ("section", "tensor")


def local(hidden, norm_gain, targets, out_weight):
    n_ten = lax.axis_size("tensor")
    row_values = hidden.astype(jnp.float32)
    inv_rms = lax.rsqrt(jnp.mean(row_values * row_values, axis=-1, keepdims=True) + 1e-05)
    normed_part = (row_values * inv_rms * norm_gain.astype(jnp.float32)[None, :]).astype(
        jnp.bfloat16
    )
    feature_width = normed_part.shape[1] // n_ten
    normed_rows = lax.dynamic_slice_in_dim(
        normed_part, lax.axis_index("tensor") * feature_width, feature_width, 1
    )
    normed = lax.all_gather(normed_part, "section", axis=0, tiled=True)
    logits = jnp.dot(normed, out_weight, preferred_element_type=jnp.float32)
    shard_width = out_weight.shape[1]
    offset = (lax.axis_index("section") * n_ten + lax.axis_index("tensor")) * shard_width
    columns = offset + lax.iota(jnp.int32, shard_width)
    target_hits = (targets[:, None] == columns[None, :]).astype(jnp.float32)
    own_target = jnp.sum(logits * target_hits, axis=1)
    local_peak = jnp.max(logits, axis=1)
    local_total = jnp.sum(jnp.exp(logits - local_peak[:, None]), axis=1)
    stats = jnp.stack([local_peak, local_total, own_target])
    with jax.named_scope("softmax_stats_gather"):
        every = lax.all_gather(stats, ALL, axis=0)
    row_peak = jnp.max(every[:, 0], axis=0)
    row_total = jnp.sum(every[:, 1] * jnp.exp(every[:, 0] - row_peak[None, :]), axis=0)
    target_logit = jnp.sum(every[:, 2], axis=0)
    token_loss = row_peak + jnp.log(row_total) - target_logit
    weights = jnp.exp(logits - row_peak[:, None])
    shares = weights / row_total[:, None]
    probs = shares.astype(jnp.bfloat16)
    grad_logits = (shares - target_hits).astype(jnp.bfloat16)
    grad_weight = lax.dot_general(
        normed, probs, (((0,), (0,)), ((), ())), preferred_element_type=jnp.float32
    ).astype(jnp.bfloat16)
    grad_term = lax.dot_general(
        grad_logits, out_weight, (((1,), (1,)), ((), ())), preferred_element_type=jnp.float32
    )
    with jax.named_scope("grad_rows_reduce_scatter"):
        partial_value = lax.psum_scatter(grad_term, "tensor", scatter_dimension=1, tiled=True)
        grad_normed = lax.psum_scatter(partial_value, "section", scatter_dimension=0, tiled=True)
    return (token_loss, grad_normed.astype(jnp.bfloat16), grad_weight, normed_rows)


def solution(mesh):
    placed = (P("section", None), P(), P(), P(None, ("section", "tensor")))
    return jax.shard_map(
        local,
        mesh=mesh,
        in_specs=placed,
        out_specs=(
            P(),
            P("section", "tensor"),
            P(None, ("section", "tensor")),
            P("section", "tensor"),
        ),
        check_vma=False,
    )
```

```python
import jax
import jax.numpy as jnp
from jax import lax
from jax.sharding import PartitionSpec as P

ALL = ("section", "tensor")


def shifted_pairs(size, stride, count, shift):
    pairs = []
    for index in range(size):
        coord = (index // stride) % count
        pairs.append((index, index + ((coord + shift) % count - coord) * stride))
    return pairs


def gather_along(value, name, stride, count):
    size = lax.axis_size(name)
    coord = (lax.axis_index(name) // stride) % count
    received = [value]
    for shift in range(1, count):
        received.append(lax.ppermute(value, name, shifted_pairs(size, stride, count, shift)))
    stacked = jnp.stack(received)
    order = (coord - jnp.arange(count, dtype=jnp.int32)) % count
    return jnp.take(stacked, order, axis=0)


def merge_stats(every):
    peak = jnp.max(every[:, 0], axis=0)
    total = jnp.sum(every[:, 1] * jnp.exp(every[:, 0] - peak[None, :]), axis=0)
    target = jnp.sum(every[:, 2], axis=0)
    return jnp.stack([peak, total, target])


def local(hidden, norm_gain, targets, out_weight):
    n_ten = lax.axis_size("tensor")
    row_values = hidden.astype(jnp.float32)
    inv_rms = lax.rsqrt(jnp.mean(row_values * row_values, axis=-1, keepdims=True) + 1e-05)
    normed_part = (row_values * inv_rms * norm_gain.astype(jnp.float32)[None, :]).astype(
        jnp.bfloat16
    )
    feature_width = normed_part.shape[1] // n_ten
    normed_rows = lax.dynamic_slice_in_dim(
        normed_part, lax.axis_index("tensor") * feature_width, feature_width, 1
    )
    normed = lax.all_gather(normed_part, "section", axis=0, tiled=True)
    logits = jnp.dot(normed, out_weight, preferred_element_type=jnp.float32)
    shard_width = out_weight.shape[1]
    offset = (lax.axis_index("section") * n_ten + lax.axis_index("tensor")) * shard_width
    columns = offset + lax.iota(jnp.int32, shard_width)
    target_hits = (targets[:, None] == columns[None, :]).astype(jnp.float32)
    own_target = jnp.sum(logits * target_hits, axis=1)
    local_peak = jnp.max(logits, axis=1)
    local_total = jnp.sum(jnp.exp(logits - local_peak[:, None]), axis=1)
    stats = jnp.stack([local_peak, local_total, own_target])
    with jax.named_scope("softmax_stats_exchange"):
        for stride, count in ((1, 2), (2, 8), (16, 4)):
            stats = merge_stats(gather_along(stats, "tensor", stride, count))
        stats = merge_stats(gather_along(stats, "section", 1, lax.axis_size("section")))
    row_peak, row_total, target_logit = stats[0], stats[1], stats[2]
    token_loss = row_peak + jnp.log(row_total) - target_logit
    weights = jnp.exp(logits - row_peak[:, None])
    shares = weights / row_total[:, None]
    probs = shares.astype(jnp.bfloat16)
    grad_logits = (shares - target_hits).astype(jnp.bfloat16)
    grad_weight = lax.dot_general(
        normed, probs, (((0,), (0,)), ((), ())), preferred_element_type=jnp.float32
    ).astype(jnp.bfloat16)
    grad_term = lax.dot_general(
        grad_logits, out_weight, (((1,), (1,)), ((), ())), preferred_element_type=jnp.float32
    )
    with jax.named_scope("grad_rows_reduce_scatter"):
        partial_value = lax.psum_scatter(grad_term, "tensor", scatter_dimension=1, tiled=True)
    with jax.named_scope("grad_rows_section_exchange"):
        n_sec = lax.axis_size("section")
        sec = lax.axis_index("section")
        blocks = partial_value.reshape(n_sec, partial_value.shape[0] // n_sec, partial_value.shape[1])
        grad_normed = lax.dynamic_index_in_dim(blocks, sec, 0, keepdims=False)
        for shift in range(1, n_sec):
            sent = lax.dynamic_index_in_dim(blocks, (sec + shift) % n_sec, 0, keepdims=False)
            pairs = [(i, (i + shift) % n_sec) for i in range(n_sec)]
            grad_normed = grad_normed + lax.ppermute(sent, "section", pairs)
    return (token_loss, grad_normed.astype(jnp.bfloat16), grad_weight, normed_rows)


def solution(mesh):
    placed = (P("section", None), P(), P(), P(None, ("section", "tensor")))
    return jax.shard_map(
        local,
        mesh=mesh,
        in_specs=placed,
        out_specs=(
            P(),
            P("section", "tensor"),
            P(None, ("section", "tensor")),
            P("section", "tensor"),
        ),
        check_vma=False,
    )
```

```python
import jax
import jax.numpy as jnp
from jax import lax
from jax.sharding import PartitionSpec as P

TENSOR_MASK_ORDER = (1, 2, 16, 4, 32, 8)


def split_pow2(count):
    low = 1
    while count % (low * 2) == 0:
        low *= 2
    return low, count // low


def tensor_masks(count):
    masks = [m for m in TENSOR_MASK_ORDER if m < count]
    masks += [1 << j for j in range(count.bit_length() - 1) if (1 << j) not in masks]
    return masks


def section_masks(count):
    low, _ = split_pow2(count)
    return [1 << j for j in range(low.bit_length() - 1)]


def xor_pairs(count, mask):
    return [(i, i ^ mask) for i in range(count)]


def merge_pair(first, second):
    peak = jnp.maximum(first[0], second[0])
    total = first[1] * jnp.exp(first[0] - peak) + second[1] * jnp.exp(second[0] - peak)
    return jnp.stack([peak, total, first[2] + second[2]])


def merge_stats(every):
    peak = jnp.max(every[:, 0], axis=0)
    total = jnp.sum(every[:, 1] * jnp.exp(every[:, 0] - peak[None, :]), axis=0)
    target = jnp.sum(every[:, 2], axis=0)
    return jnp.stack([peak, total, target])


def exchange_stats(stats):
    steps = [("tensor", m) for m in tensor_masks(lax.axis_size("tensor"))]
    steps += [("section", m) for m in section_masks(lax.axis_size("section"))]
    for name, mask in steps:
        other = lax.ppermute(stats, name, xor_pairs(lax.axis_size(name), mask))
        upper = (lax.axis_index(name) & mask) != 0
        stats = merge_pair(jnp.where(upper, other, stats), jnp.where(upper, stats, other))
    n_sec = lax.axis_size("section")
    low, groups = split_pow2(n_sec)
    if groups > 1:
        group = lax.axis_index("section") // low
        received = [stats]
        for shift in range(1, groups):
            pairs = [(i, (i + shift * low) % n_sec) for i in range(n_sec)]
            received.append(lax.ppermute(stats, "section", pairs))
        order = (group - jnp.arange(groups, dtype=jnp.int32)) % groups
        stats = merge_stats(jnp.take(jnp.stack(received), order, axis=0))
    return stats


def reduce_scatter_blocks(blocks):
    n_sec, n_ten = blocks.shape[0], blocks.shape[1]
    low, groups = split_pow2(n_sec)
    t_bits = n_ten.bit_length() - 1
    s_bits = low.bit_length() - 1
    labels = ["group"] + [("section", 1 << j) for j in reversed(range(s_bits))]
    labels += [("tensor", 1 << j) for j in reversed(range(t_bits))]
    value = blocks.reshape((groups,) + (2,) * (s_bits + t_bits) + blocks.shape[2:])
    steps = [("tensor", m) for m in tensor_masks(n_ten)] + [("section", m) for m in section_masks(n_sec)]
    for name, mask in steps:
        axis = labels.index((name, mask))
        mine = (lax.axis_index(name) & mask) // mask
        keep = lax.dynamic_index_in_dim(value, mine, axis, keepdims=False)
        sent = lax.dynamic_index_in_dim(value, 1 - mine, axis, keepdims=False)
        value = keep + lax.ppermute(sent, name, xor_pairs(lax.axis_size(name), mask))
        labels.pop(axis)
    group = lax.axis_index("section") // low
    total = lax.dynamic_index_in_dim(value, group, 0, keepdims=False)
    for shift in range(1, groups):
        sent = lax.dynamic_index_in_dim(value, (group + shift) % groups, 0, keepdims=False)
        pairs = [(i, (i + shift * low) % n_sec) for i in range(n_sec)]
        total = total + lax.ppermute(sent, "section", pairs)
    return total


def local(hidden, norm_gain, targets, out_weight):
    n_sec = lax.axis_size("section")
    n_ten = lax.axis_size("tensor")
    row_values = hidden.astype(jnp.float32)
    inv_rms = lax.rsqrt(jnp.mean(row_values * row_values, axis=-1, keepdims=True) + 1e-05)
    normed_part = (row_values * inv_rms * norm_gain.astype(jnp.float32)[None, :]).astype(
        jnp.bfloat16
    )
    rows_per_sec = normed_part.shape[0]
    feature_width = normed_part.shape[1] // n_ten
    normed_rows = lax.dynamic_slice_in_dim(
        normed_part, lax.axis_index("tensor") * feature_width, feature_width, 1
    )
    normed = lax.all_gather(normed_part, "section", axis=0, tiled=True)
    logits = jnp.dot(normed, out_weight, preferred_element_type=jnp.float32)
    shard_width = out_weight.shape[1]
    offset = (lax.axis_index("section") * n_ten + lax.axis_index("tensor")) * shard_width
    columns = offset + lax.iota(jnp.int32, shard_width)
    target_hits = (targets[:, None] == columns[None, :]).astype(jnp.float32)
    own_target = jnp.sum(logits * target_hits, axis=1)
    local_peak = jnp.max(logits, axis=1)
    local_total = jnp.sum(jnp.exp(logits - local_peak[:, None]), axis=1)
    with jax.named_scope("softmax_stats_exchange"):
        stats = exchange_stats(jnp.stack([local_peak, local_total, own_target]))
    row_peak, row_total, target_logit = stats[0], stats[1], stats[2]
    token_loss = row_peak + jnp.log(row_total) - target_logit
    weights = jnp.exp(logits - row_peak[:, None])
    shares = weights / row_total[:, None]
    probs = shares.astype(jnp.bfloat16)
    grad_logits = (shares - target_hits).astype(jnp.bfloat16)
    grad_weight = lax.dot_general(
        normed, probs, (((0,), (0,)), ((), ())), preferred_element_type=jnp.float32
    ).astype(jnp.bfloat16)
    grad_term = lax.dot_general(
        grad_logits, out_weight, (((1,), (1,)), ((), ())), preferred_element_type=jnp.float32
    )
    blocks = grad_term.reshape(n_sec, rows_per_sec, n_ten, feature_width).transpose(0, 2, 1, 3)
    with jax.named_scope("grad_rows_reduce_scatter"):
        grad_normed = reduce_scatter_blocks(blocks)
    return (token_loss, grad_normed.astype(jnp.bfloat16), grad_weight, normed_rows)


def solution(mesh):
    placed = (P("section", None), P(), P(), P(None, ("section", "tensor")))
    return jax.shard_map(
        local,
        mesh=mesh,
        in_specs=placed,
        out_specs=(
            P(),
            P("section", "tensor"),
            P(None, ("section", "tensor")),
            P("section", "tensor"),
        ),
        check_vma=False,
    )
```

```python
import jax
import jax.numpy as jnp
from jax import lax
from jax.sharding import PartitionSpec as P

TENSOR_MASK_ORDER = (1, 2, 16, 4, 32, 8)


def tensor_geometry(count):
    along_y = min(8, count // 2)
    return count // 2 // along_y, along_y


def labelled(index, count):
    n_x, n_y = tensor_geometry(count)
    core, chip = index % 2, index // 2
    x, y = chip // n_y, chip % n_y
    return ((x + core) % n_x * n_y + (y + core) % n_y) * 2 + core


def unlabelled(label, count):
    n_x, n_y = tensor_geometry(count)
    core, chip = label % 2, label // 2
    x, y = chip // n_y, chip % n_y
    return ((x - core) % n_x * n_y + (y - core) % n_y) * 2 + core


def split_pow2(count):
    low = 1
    while count % (low * 2) == 0:
        low *= 2
    return low, count // low


def tensor_masks(count):
    masks = [m for m in TENSOR_MASK_ORDER if m < count]
    masks += [1 << j for j in range(count.bit_length() - 1) if (1 << j) not in masks]
    return masks


def section_masks(count):
    low, _ = split_pow2(count)
    return [1 << j for j in range(low.bit_length() - 1)]


def xor_pairs(count, mask):
    return [(i, i ^ mask) for i in range(count)]


def merge_pair(first, second):
    peak = jnp.maximum(first[0], second[0])
    total = first[1] * jnp.exp(first[0] - peak) + second[1] * jnp.exp(second[0] - peak)
    return jnp.stack([peak, total, first[2] + second[2]])


def merge_stats(every):
    peak = jnp.max(every[:, 0], axis=0)
    total = jnp.sum(every[:, 1] * jnp.exp(every[:, 0] - peak[None, :]), axis=0)
    target = jnp.sum(every[:, 2], axis=0)
    return jnp.stack([peak, total, target])


def exchange_stats(stats):
    steps = [("tensor", m) for m in tensor_masks(lax.axis_size("tensor"))]
    steps += [("section", m) for m in section_masks(lax.axis_size("section"))]
    for name, mask in steps:
        other = lax.ppermute(stats, name, xor_pairs(lax.axis_size(name), mask))
        upper = (lax.axis_index(name) & mask) != 0
        stats = merge_pair(jnp.where(upper, other, stats), jnp.where(upper, stats, other))
    n_sec = lax.axis_size("section")
    low, groups = split_pow2(n_sec)
    if groups > 1:
        group = lax.axis_index("section") // low
        received = [stats]
        for shift in range(1, groups):
            pairs = [(i, (i + shift * low) % n_sec) for i in range(n_sec)]
            received.append(lax.ppermute(stats, "section", pairs))
        order = (group - jnp.arange(groups, dtype=jnp.int32)) % groups
        stats = merge_stats(jnp.take(jnp.stack(received), order, axis=0))
    return stats


def reduce_scatter_blocks(blocks):
    n_sec, n_ten = blocks.shape[0], blocks.shape[1]
    low, groups = split_pow2(n_sec)
    t_bits = n_ten.bit_length() - 1
    s_bits = low.bit_length() - 1
    labels = ["group"] + [("section", 1 << j) for j in reversed(range(s_bits))]
    labels += [("tensor", 1 << j) for j in reversed(range(t_bits))]
    n_x, n_y = tensor_geometry(n_ten)
    chips = blocks.reshape((n_sec, n_x, n_y, 2) + blocks.shape[2:])
    shifted = jnp.roll(chips[:, :, :, 1], shift=(1, 1), axis=(1, 2))
    chips = jnp.stack([chips[:, :, :, 0], shifted], axis=3)
    value = chips.reshape((groups,) + (2,) * (s_bits + t_bits) + blocks.shape[2:])
    steps = [("tensor", m) for m in tensor_masks(n_ten)] + [("section", m) for m in section_masks(n_sec)]
    t = lax.axis_index("tensor")
    core = t % 2
    chip = t // 2
    t_label = (((chip // n_y) + core) % n_x * n_y + ((chip % n_y) + core) % n_y) * 2 + core
    for name, mask in steps:
        axis = labels.index((name, mask))
        size = lax.axis_size(name)
        if name == "tensor":
            mine = (t_label & mask) // mask
            pairs = [(i, unlabelled(labelled(i, size) ^ mask, size)) for i in range(size)]
        else:
            mine = (lax.axis_index(name) & mask) // mask
            pairs = xor_pairs(size, mask)
        keep = lax.dynamic_index_in_dim(value, mine, axis, keepdims=False)
        sent = lax.dynamic_index_in_dim(value, 1 - mine, axis, keepdims=False)
        value = keep + lax.ppermute(sent, name, pairs)
        labels.pop(axis)
    group = lax.axis_index("section") // low
    total = lax.dynamic_index_in_dim(value, group, 0, keepdims=False)
    for shift in range(1, groups):
        sent = lax.dynamic_index_in_dim(value, (group + shift) % groups, 0, keepdims=False)
        pairs = [(i, (i + shift * low) % n_sec) for i in range(n_sec)]
        total = total + lax.ppermute(sent, "section", pairs)
    return total


def local(hidden, norm_gain, targets, out_weight):
    n_sec = lax.axis_size("section")
    n_ten = lax.axis_size("tensor")
    row_values = hidden.astype(jnp.float32)
    inv_rms = lax.rsqrt(jnp.mean(row_values * row_values, axis=-1, keepdims=True) + 1e-05)
    normed_part = (row_values * inv_rms * norm_gain.astype(jnp.float32)[None, :]).astype(
        jnp.bfloat16
    )
    rows_per_sec = normed_part.shape[0]
    feature_width = normed_part.shape[1] // n_ten
    normed_rows = lax.dynamic_slice_in_dim(
        normed_part, lax.axis_index("tensor") * feature_width, feature_width, 1
    )
    core = lax.axis_index("tensor") % 2
    half = normed_part.shape[1] // 2
    with jax.named_scope("normed_rows_gather"):
        own_half = lax.all_gather(
            lax.dynamic_slice_in_dim(normed_part, core * half, half, 1), "section", axis=0, tiled=True
        )
        other_half = lax.ppermute(own_half, "tensor", xor_pairs(n_ten, 1))
    normed = jnp.where(
        core == 0,
        jnp.concatenate([own_half, other_half], axis=1),
        jnp.concatenate([other_half, own_half], axis=1),
    )
    logits = jnp.dot(normed, out_weight, preferred_element_type=jnp.float32)
    shard_width = out_weight.shape[1]
    offset = (lax.axis_index("section") * n_ten + lax.axis_index("tensor")) * shard_width
    columns = offset + lax.iota(jnp.int32, shard_width)
    target_hits = (targets[:, None] == columns[None, :]).astype(jnp.float32)
    own_target = jnp.sum(logits * target_hits, axis=1)
    local_peak = jnp.max(logits, axis=1)
    local_total = jnp.sum(jnp.exp(logits - local_peak[:, None]), axis=1)
    with jax.named_scope("softmax_stats_exchange"):
        stats = exchange_stats(jnp.stack([local_peak, local_total, own_target]))
    row_peak, row_total, target_logit = stats[0], stats[1], stats[2]
    token_loss = row_peak + jnp.log(row_total) - target_logit
    weights = jnp.exp(logits - row_peak[:, None])
    shares = weights / row_total[:, None]
    probs = shares.astype(jnp.bfloat16)
    grad_logits = (shares - target_hits).astype(jnp.bfloat16)
    grad_weight = lax.dot_general(
        normed, probs, (((0,), (0,)), ((), ())), preferred_element_type=jnp.float32
    ).astype(jnp.bfloat16)
    grad_term = lax.dot_general(
        grad_logits, out_weight, (((1,), (1,)), ((), ())), preferred_element_type=jnp.float32
    )
    blocks = grad_term.reshape(n_sec, rows_per_sec, n_ten, feature_width).transpose(0, 2, 1, 3)
    with jax.named_scope("grad_rows_reduce_scatter"):
        grad_normed = reduce_scatter_blocks(blocks)
    return (token_loss, grad_normed.astype(jnp.bfloat16), grad_weight, normed_rows)


def solution(mesh):
    placed = (P("section", None), P(), P(), P(None, ("section", "tensor")))
    return jax.shard_map(
        local,
        mesh=mesh,
        in_specs=placed,
        out_specs=(
            P(),
            P("section", "tensor"),
            P(None, ("section", "tensor")),
            P("section", "tensor"),
        ),
        check_vma=False,
    )
```

```python
import jax
import jax.numpy as jnp
from jax import lax
from jax.sharding import PartitionSpec as P

TENSOR_MASK_ORDER = (1, 2, 16, 4, 32, 8)
SPLIT_BYTES = 256 * 1024


def split_pow2(count):
    low = 1
    while count % (low * 2) == 0:
        low *= 2
    return low, count // low


def tensor_masks(count):
    masks = [m for m in TENSOR_MASK_ORDER if m < count]
    masks += [1 << j for j in range(count.bit_length() - 1) if (1 << j) not in masks]
    return masks


def section_masks(count):
    low, _ = split_pow2(count)
    return [1 << j for j in range(low.bit_length() - 1)]


def xor_pairs(count, mask):
    return [(i, i ^ mask) for i in range(count)]


def merge_pair(first, second):
    peak = jnp.maximum(first[0], second[0])
    total = first[1] * jnp.exp(first[0] - peak) + second[1] * jnp.exp(second[0] - peak)
    return jnp.stack([peak, total, first[2] + second[2]])


def merge_stats(every):
    peak = jnp.max(every[:, 0], axis=0)
    total = jnp.sum(every[:, 1] * jnp.exp(every[:, 0] - peak[None, :]), axis=0)
    target = jnp.sum(every[:, 2], axis=0)
    return jnp.stack([peak, total, target])


def exchange_stats(stats):
    steps = [("tensor", m) for m in tensor_masks(lax.axis_size("tensor"))]
    steps += [("section", m) for m in section_masks(lax.axis_size("section"))]
    for name, mask in steps:
        other = lax.ppermute(stats, name, xor_pairs(lax.axis_size(name), mask))
        upper = (lax.axis_index(name) & mask) != 0
        stats = merge_pair(jnp.where(upper, other, stats), jnp.where(upper, stats, other))
    n_sec = lax.axis_size("section")
    low, groups = split_pow2(n_sec)
    if groups > 1:
        group = lax.axis_index("section") // low
        received = [stats]
        for shift in range(1, groups):
            pairs = [(i, (i + shift * low) % n_sec) for i in range(n_sec)]
            received.append(lax.ppermute(stats, "section", pairs))
        order = (group - jnp.arange(groups, dtype=jnp.int32)) % groups
        stats = merge_stats(jnp.take(jnp.stack(received), order, axis=0))
    return stats


def reduce_scatter_blocks(blocks):
    n_sec, n_ten = blocks.shape[0], blocks.shape[1]
    low, groups = split_pow2(n_sec)
    t_bits = n_ten.bit_length() - 1
    s_bits = low.bit_length() - 1
    labels = ["group"] + [("section", 1 << j) for j in reversed(range(s_bits))]
    labels += [("tensor", 1 << j) for j in reversed(range(t_bits))]
    value = blocks.reshape((groups,) + (2,) * (s_bits + t_bits) + blocks.shape[2:])
    steps = [("tensor", m) for m in tensor_masks(n_ten)] + [("section", m) for m in section_masks(n_sec)]
    for name, mask in steps:
        axis = labels.index((name, mask))
        mine = (lax.axis_index(name) & mask) // mask
        keep = lax.dynamic_index_in_dim(value, mine, axis, keepdims=False)
        sent = lax.dynamic_index_in_dim(value, 1 - mine, axis, keepdims=False)
        pairs = xor_pairs(lax.axis_size(name), mask)
        if name == "tensor" and mask != 1 and sent.size * 4 >= SPLIT_BYTES:
            rows = sent.shape[-2] // 2
            halves = [lax.slice_in_dim(sent, i * rows, (i + 1) * rows, axis=sent.ndim - 2) for i in range(2)]
            sent_back = jnp.concatenate([lax.ppermute(h, name, pairs) for h in halves], axis=sent.ndim - 2)
        else:
            sent_back = lax.ppermute(sent, name, pairs)
        value = keep + sent_back
        labels.pop(axis)
    group = lax.axis_index("section") // low
    total = lax.dynamic_index_in_dim(value, group, 0, keepdims=False)
    for shift in range(1, groups):
        sent = lax.dynamic_index_in_dim(value, (group + shift) % groups, 0, keepdims=False)
        pairs = [(i, (i + shift * low) % n_sec) for i in range(n_sec)]
        total = total + lax.ppermute(sent, "section", pairs)
    return total


def local(hidden, norm_gain, targets, out_weight):
    n_sec = lax.axis_size("section")
    n_ten = lax.axis_size("tensor")
    row_values = hidden.astype(jnp.float32)
    inv_rms = lax.rsqrt(jnp.mean(row_values * row_values, axis=-1, keepdims=True) + 1e-05)
    normed_part = (row_values * inv_rms * norm_gain.astype(jnp.float32)[None, :]).astype(
        jnp.bfloat16
    )
    rows_per_sec = normed_part.shape[0]
    feature_width = normed_part.shape[1] // n_ten
    normed_rows = lax.dynamic_slice_in_dim(
        normed_part, lax.axis_index("tensor") * feature_width, feature_width, 1
    )
    normed = lax.all_gather(normed_part, "section", axis=0, tiled=True)
    logits = jnp.dot(normed, out_weight, preferred_element_type=jnp.float32)
    shard_width = out_weight.shape[1]
    offset = (lax.axis_index("section") * n_ten + lax.axis_index("tensor")) * shard_width
    columns = offset + lax.iota(jnp.int32, shard_width)
    target_hits = (targets[:, None] == columns[None, :]).astype(jnp.float32)
    own_target = jnp.sum(logits * target_hits, axis=1)
    local_peak = jnp.max(logits, axis=1)
    local_total = jnp.sum(jnp.exp(logits - local_peak[:, None]), axis=1)
    with jax.named_scope("softmax_stats_exchange"):
        stats = exchange_stats(jnp.stack([local_peak, local_total, own_target]))
    row_peak, row_total, target_logit = stats[0], stats[1], stats[2]
    token_loss = row_peak + jnp.log(row_total) - target_logit
    weights = jnp.exp(logits - row_peak[:, None])
    shares = weights / row_total[:, None]
    probs = shares.astype(jnp.bfloat16)
    grad_logits = (shares - target_hits).astype(jnp.bfloat16)
    grad_weight = lax.dot_general(
        normed, probs, (((0,), (0,)), ((), ())), preferred_element_type=jnp.float32
    ).astype(jnp.bfloat16)
    grad_term = lax.dot_general(
        grad_logits, out_weight, (((1,), (1,)), ((), ())), preferred_element_type=jnp.float32
    )
    blocks = grad_term.reshape(n_sec, rows_per_sec, n_ten, feature_width).transpose(0, 2, 1, 3)
    with jax.named_scope("grad_rows_reduce_scatter"):
        grad_normed = reduce_scatter_blocks(blocks)
    return (token_loss, grad_normed.astype(jnp.bfloat16), grad_weight, normed_rows)


def solution(mesh):
    placed = (P("section", None), P(), P(), P(None, ("section", "tensor")))
    return jax.shard_map(
        local,
        mesh=mesh,
        in_specs=placed,
        out_specs=(
            P(),
            P("section", "tensor"),
            P(None, ("section", "tensor")),
            P("section", "tensor"),
        ),
        check_vma=False,
    )
```

```python
import jax
import jax.numpy as jnp
from jax import lax
from jax.sharding import PartitionSpec as P

TENSOR_MASK_ORDER = (1, 2, 16, 4, 32, 8)


def split_pow2(count):
    low = 1
    while count % (low * 2) == 0:
        low *= 2
    return low, count // low


def tensor_masks(count):
    masks = [m for m in TENSOR_MASK_ORDER if m < count]
    masks += [1 << j for j in range(count.bit_length() - 1) if (1 << j) not in masks]
    return masks


def section_masks(count):
    low, _ = split_pow2(count)
    return [1 << j for j in range(low.bit_length() - 1)]


def xor_pairs(count, mask):
    return [(i, i ^ mask) for i in range(count)]


def merge_pair(first, second):
    peak = jnp.maximum(first[0], second[0])
    total = first[1] * jnp.exp(first[0] - peak) + second[1] * jnp.exp(second[0] - peak)
    return jnp.stack([peak, total, first[2] + second[2]])


def merge_stats(every):
    peak = jnp.max(every[:, 0], axis=0)
    total = jnp.sum(every[:, 1] * jnp.exp(every[:, 0] - peak[None, :]), axis=0)
    target = jnp.sum(every[:, 2], axis=0)
    return jnp.stack([peak, total, target])


def exchange_stats(stats):
    steps = [("tensor", m) for m in tensor_masks(lax.axis_size("tensor"))]
    steps += [("section", m) for m in section_masks(lax.axis_size("section"))]
    for name, mask in steps:
        other = lax.ppermute(stats, name, xor_pairs(lax.axis_size(name), mask))
        upper = (lax.axis_index(name) & mask) != 0
        stats = merge_pair(jnp.where(upper, other, stats), jnp.where(upper, stats, other))
    n_sec = lax.axis_size("section")
    low, groups = split_pow2(n_sec)
    if groups > 1:
        group = lax.axis_index("section") // low
        received = [stats]
        for shift in range(1, groups):
            pairs = [(i, (i + shift * low) % n_sec) for i in range(n_sec)]
            received.append(lax.ppermute(stats, "section", pairs))
        order = (group - jnp.arange(groups, dtype=jnp.int32)) % groups
        stats = merge_stats(jnp.take(jnp.stack(received), order, axis=0))
    return stats


def reduce_scatter_blocks(blocks):
    n_sec, n_ten = blocks.shape[0], blocks.shape[1]
    low, groups = split_pow2(n_sec)
    t_bits = n_ten.bit_length() - 1
    s_bits = low.bit_length() - 1
    labels = ["group"] + [("section", 1 << j) for j in reversed(range(s_bits))]
    labels += [("tensor", 1 << j) for j in reversed(range(t_bits))]
    value = blocks.reshape((groups,) + (2,) * (s_bits + t_bits) + blocks.shape[2:])
    t_steps = [("tensor", m) for m in tensor_masks(n_ten)]
    s_steps = [("section", m) for m in section_masks(n_sec)]
    steps = t_steps[:3] + s_steps[:1] + t_steps[3:5] + s_steps[1:2] + t_steps[5:] + s_steps[2:]
    for name, mask in steps:
        axis = labels.index((name, mask))
        mine = (lax.axis_index(name) & mask) // mask
        keep = lax.dynamic_index_in_dim(value, mine, axis, keepdims=False)
        sent = lax.dynamic_index_in_dim(value, 1 - mine, axis, keepdims=False)
        value = keep + lax.ppermute(sent, name, xor_pairs(lax.axis_size(name), mask))
        labels.pop(axis)
    group = lax.axis_index("section") // low
    total = lax.dynamic_index_in_dim(value, group, 0, keepdims=False)
    for shift in range(1, groups):
        sent = lax.dynamic_index_in_dim(value, (group + shift) % groups, 0, keepdims=False)
        pairs = [(i, (i + shift * low) % n_sec) for i in range(n_sec)]
        total = total + lax.ppermute(sent, "section", pairs)
    return total


def local(hidden, norm_gain, targets, out_weight):
    n_sec = lax.axis_size("section")
    n_ten = lax.axis_size("tensor")
    row_values = hidden.astype(jnp.float32)
    inv_rms = lax.rsqrt(jnp.mean(row_values * row_values, axis=-1, keepdims=True) + 1e-05)
    normed_part = (row_values * inv_rms * norm_gain.astype(jnp.float32)[None, :]).astype(
        jnp.bfloat16
    )
    rows_per_sec = normed_part.shape[0]
    feature_width = normed_part.shape[1] // n_ten
    normed_rows = lax.dynamic_slice_in_dim(
        normed_part, lax.axis_index("tensor") * feature_width, feature_width, 1
    )
    normed = lax.all_gather(normed_part, "section", axis=0, tiled=True)
    logits = jnp.dot(normed, out_weight, preferred_element_type=jnp.float32)
    shard_width = out_weight.shape[1]
    offset = (lax.axis_index("section") * n_ten + lax.axis_index("tensor")) * shard_width
    columns = offset + lax.iota(jnp.int32, shard_width)
    target_hits = (targets[:, None] == columns[None, :]).astype(jnp.float32)
    own_target = jnp.sum(logits * target_hits, axis=1)
    local_peak = jnp.max(logits, axis=1)
    local_total = jnp.sum(jnp.exp(logits - local_peak[:, None]), axis=1)
    with jax.named_scope("softmax_stats_exchange"):
        stats = exchange_stats(jnp.stack([local_peak, local_total, own_target]))
    row_peak, row_total, target_logit = stats[0], stats[1], stats[2]
    token_loss = row_peak + jnp.log(row_total) - target_logit
    weights = jnp.exp(logits - row_peak[:, None])
    shares = weights / row_total[:, None]
    probs = shares.astype(jnp.bfloat16)
    grad_logits = (shares - target_hits).astype(jnp.bfloat16)
    grad_weight = lax.dot_general(
        normed, probs, (((0,), (0,)), ((), ())), preferred_element_type=jnp.float32
    ).astype(jnp.bfloat16)
    grad_term = lax.dot_general(
        grad_logits, out_weight, (((1,), (1,)), ((), ())), preferred_element_type=jnp.float32
    )
    blocks = grad_term.reshape(n_sec, rows_per_sec, n_ten, feature_width).transpose(0, 2, 1, 3)
    with jax.named_scope("grad_rows_reduce_scatter"):
        grad_normed = reduce_scatter_blocks(blocks)
    return (token_loss, grad_normed.astype(jnp.bfloat16), grad_weight, normed_rows)


def solution(mesh):
    placed = (P("section", None), P(), P(), P(None, ("section", "tensor")))
    return jax.shard_map(
        local,
        mesh=mesh,
        in_specs=placed,
        out_specs=(
            P(),
            P("section", "tensor"),
            P(None, ("section", "tensor")),
            P("section", "tensor"),
        ),
        check_vma=False,
    )
```

```python
import jax
import jax.numpy as jnp
from jax import lax
from jax.sharding import PartitionSpec as P

TENSOR_MASK_ORDER = (1, 2, 16, 4, 32, 8)


def split_pow2(count):
    low = 1
    while count % (low * 2) == 0:
        low *= 2
    return low, count // low


def tensor_masks(count):
    masks = [m for m in TENSOR_MASK_ORDER if m < count]
    masks += [1 << j for j in range(count.bit_length() - 1) if (1 << j) not in masks]
    return masks


def section_masks(count):
    low, _ = split_pow2(count)
    return [1 << j for j in range(low.bit_length() - 1)]


def xor_pairs(count, mask):
    return [(i, i ^ mask) for i in range(count)]


def merge_pair(first, second):
    peak = jnp.maximum(first[0], second[0])
    total = first[1] * jnp.exp(first[0] - peak) + second[1] * jnp.exp(second[0] - peak)
    return jnp.stack([peak, total, first[2] + second[2]])


def merge_stats(every):
    peak = jnp.max(every[:, 0], axis=0)
    total = jnp.sum(every[:, 1] * jnp.exp(every[:, 0] - peak[None, :]), axis=0)
    target = jnp.sum(every[:, 2], axis=0)
    return jnp.stack([peak, total, target])


def exchange_stats(stats):
    steps = [("tensor", m) for m in tensor_masks(lax.axis_size("tensor"))]
    steps += [("section", m) for m in section_masks(lax.axis_size("section"))]
    for name, mask in steps:
        other = lax.ppermute(stats, name, xor_pairs(lax.axis_size(name), mask))
        upper = (lax.axis_index(name) & mask) != 0
        stats = merge_pair(jnp.where(upper, other, stats), jnp.where(upper, stats, other))
    n_sec = lax.axis_size("section")
    low, groups = split_pow2(n_sec)
    if groups > 1:
        group = lax.axis_index("section") // low
        received = [stats]
        for shift in range(1, groups):
            pairs = [(i, (i + shift * low) % n_sec) for i in range(n_sec)]
            received.append(lax.ppermute(stats, "section", pairs))
        order = (group - jnp.arange(groups, dtype=jnp.int32)) % groups
        stats = merge_stats(jnp.take(jnp.stack(received), order, axis=0))
    return stats


def reduce_scatter_blocks(blocks, rider):
    n_sec, n_ten = blocks.shape[0], blocks.shape[1]
    low, groups = split_pow2(n_sec)
    t_bits = n_ten.bit_length() - 1
    s_bits = low.bit_length() - 1
    labels = ["group"] + [("section", 1 << j) for j in reversed(range(s_bits))]
    labels += [("tensor", 1 << j) for j in reversed(range(t_bits))]
    value = blocks.reshape((groups,) + (2,) * (s_bits + t_bits) + blocks.shape[2:])
    t_steps = [("tensor", m) for m in tensor_masks(n_ten)]
    s_steps = [("section", m) for m in section_masks(n_sec)]
    steps = t_steps[:3] + s_steps[:1] + t_steps[3:5] + s_steps[1:2] + t_steps[5:] + s_steps[2:]
    for name, mask in steps:
        axis = labels.index((name, mask))
        mine = (lax.axis_index(name) & mask) // mask
        keep = lax.dynamic_index_in_dim(value, mine, axis, keepdims=False)
        sent = lax.dynamic_index_in_dim(value, 1 - mine, axis, keepdims=False)
        received = lax.ppermute(sent, name, xor_pairs(lax.axis_size(name), mask))
        if (name, mask) == steps[1]:
            keep, rider = lax.optimization_barrier((keep, rider))
        value = keep + received
        labels.pop(axis)
    group = lax.axis_index("section") // low
    total = lax.dynamic_index_in_dim(value, group, 0, keepdims=False)
    for shift in range(1, groups):
        sent = lax.dynamic_index_in_dim(value, (group + shift) % groups, 0, keepdims=False)
        pairs = [(i, (i + shift * low) % n_sec) for i in range(n_sec)]
        total = total + lax.ppermute(sent, "section", pairs)
    return total, rider


def local(hidden, norm_gain, targets, out_weight):
    n_sec = lax.axis_size("section")
    n_ten = lax.axis_size("tensor")
    row_values = hidden.astype(jnp.float32)
    inv_rms = lax.rsqrt(jnp.mean(row_values * row_values, axis=-1, keepdims=True) + 1e-05)
    normed_part = (row_values * inv_rms * norm_gain.astype(jnp.float32)[None, :]).astype(
        jnp.bfloat16
    )
    rows_per_sec = normed_part.shape[0]
    feature_width = normed_part.shape[1] // n_ten
    normed_rows = lax.dynamic_slice_in_dim(
        normed_part, lax.axis_index("tensor") * feature_width, feature_width, 1
    )
    normed = lax.all_gather(normed_part, "section", axis=0, tiled=True)
    logits = jnp.dot(normed, out_weight, preferred_element_type=jnp.float32)
    shard_width = out_weight.shape[1]
    offset = (lax.axis_index("section") * n_ten + lax.axis_index("tensor")) * shard_width
    columns = offset + lax.iota(jnp.int32, shard_width)
    target_hits = (targets[:, None] == columns[None, :]).astype(jnp.float32)
    own_target = jnp.sum(logits * target_hits, axis=1)
    local_peak = jnp.max(logits, axis=1)
    local_total = jnp.sum(jnp.exp(logits - local_peak[:, None]), axis=1)
    with jax.named_scope("softmax_stats_exchange"):
        stats = exchange_stats(jnp.stack([local_peak, local_total, own_target]))
    row_peak, row_total, target_logit = stats[0], stats[1], stats[2]
    token_loss = row_peak + jnp.log(row_total) - target_logit
    weights = jnp.exp(logits - row_peak[:, None])
    shares = weights / row_total[:, None]
    probs = shares.astype(jnp.bfloat16)
    grad_logits = (shares - target_hits).astype(jnp.bfloat16)
    grad_weight = lax.dot_general(
        normed, probs, (((0,), (0,)), ((), ())), preferred_element_type=jnp.float32
    ).astype(jnp.bfloat16)
    grad_term = lax.dot_general(
        grad_logits, out_weight, (((1,), (1,)), ((), ())), preferred_element_type=jnp.float32
    )
    blocks = grad_term.reshape(n_sec, rows_per_sec, n_ten, feature_width).transpose(0, 2, 1, 3)
    with jax.named_scope("grad_rows_reduce_scatter"):
        grad_normed, grad_weight = reduce_scatter_blocks(blocks, grad_weight)
    return (token_loss, grad_normed.astype(jnp.bfloat16), grad_weight, normed_rows)


def solution(mesh):
    placed = (P("section", None), P(), P(), P(None, ("section", "tensor")))
    return jax.shard_map(
        local,
        mesh=mesh,
        in_specs=placed,
        out_specs=(
            P(),
            P("section", "tensor"),
            P(None, ("section", "tensor")),
            P("section", "tensor"),
        ),
        check_vma=False,
    )
```

```python
import jax
import jax.numpy as jnp
from jax import lax
from jax.sharding import PartitionSpec as P

TENSOR_MASK_ORDER = (1, 2, 16, 4, 32, 8)


def split_pow2(count):
    low = 1
    while count % (low * 2) == 0:
        low *= 2
    return low, count // low


def tensor_masks(count):
    masks = [m for m in TENSOR_MASK_ORDER if m < count]
    masks += [1 << j for j in range(count.bit_length() - 1) if (1 << j) not in masks]
    return masks


def section_masks(count):
    low, _ = split_pow2(count)
    return [1 << j for j in range(low.bit_length() - 1)]


def xor_pairs(count, mask):
    return [(i, i ^ mask) for i in range(count)]


def merge_pair(first, second):
    peak = jnp.maximum(first[0], second[0])
    total = first[1] * jnp.exp(first[0] - peak) + second[1] * jnp.exp(second[0] - peak)
    return jnp.stack([peak, total, first[2] + second[2]])


def merge_stats(every):
    peak = jnp.max(every[:, 0], axis=0)
    total = jnp.sum(every[:, 1] * jnp.exp(every[:, 0] - peak[None, :]), axis=0)
    target = jnp.sum(every[:, 2], axis=0)
    return jnp.stack([peak, total, target])


def exchange_stats(stats):
    steps = [("tensor", m) for m in tensor_masks(lax.axis_size("tensor"))]
    steps += [("section", m) for m in section_masks(lax.axis_size("section"))]
    for name, mask in steps:
        other = lax.ppermute(stats, name, xor_pairs(lax.axis_size(name), mask))
        upper = (lax.axis_index(name) & mask) != 0
        stats = merge_pair(jnp.where(upper, other, stats), jnp.where(upper, stats, other))
    n_sec = lax.axis_size("section")
    low, groups = split_pow2(n_sec)
    if groups > 1:
        group = lax.axis_index("section") // low
        received = [stats]
        for shift in range(1, groups):
            pairs = [(i, (i + shift * low) % n_sec) for i in range(n_sec)]
            received.append(lax.ppermute(stats, "section", pairs))
        order = (group - jnp.arange(groups, dtype=jnp.int32)) % groups
        stats = merge_stats(jnp.take(jnp.stack(received), order, axis=0))
    return stats


def reduce_scatter_blocks(blocks, rider):
    n_sec, n_ten = blocks.shape[0], blocks.shape[1]
    low, groups = split_pow2(n_sec)
    t_bits = n_ten.bit_length() - 1
    s_bits = low.bit_length() - 1
    labels = ["group"] + [("section", 1 << j) for j in reversed(range(s_bits))]
    labels += [("tensor", 1 << j) for j in reversed(range(t_bits))]
    value = blocks.reshape((groups,) + (2,) * (s_bits + t_bits) + blocks.shape[2:])
    t_steps = [("tensor", m) for m in tensor_masks(n_ten)]
    s_steps = [("section", m) for m in section_masks(n_sec)]
    steps = t_steps[:3] + s_steps[:1] + t_steps[3:5] + s_steps[1:2] + t_steps[5:] + s_steps[2:]
    for name, mask in steps:
        axis = labels.index((name, mask))
        mine = (lax.axis_index(name) & mask) // mask
        keep = lax.dynamic_index_in_dim(value, mine, axis, keepdims=False)
        sent = lax.dynamic_index_in_dim(value, 1 - mine, axis, keepdims=False)
        received = lax.ppermute(sent, name, xor_pairs(lax.axis_size(name), mask))
        if (name, mask) == steps[1]:
            keep, rider = lax.optimization_barrier((keep, rider))
        value = keep + received
        labels.pop(axis)
    group = lax.axis_index("section") // low
    total = lax.dynamic_index_in_dim(value, group, 0, keepdims=False)
    for shift in range(1, groups):
        sent = lax.dynamic_index_in_dim(value, (group + shift) % groups, 0, keepdims=False)
        pairs = [(i, (i + shift * low) % n_sec) for i in range(n_sec)]
        total = total + lax.ppermute(sent, "section", pairs)
    return total, rider


def local(hidden, norm_gain, targets, out_weight):
    n_sec = lax.axis_size("section")
    n_ten = lax.axis_size("tensor")
    row_values = hidden.astype(jnp.float32)
    inv_rms = lax.rsqrt(jnp.mean(row_values * row_values, axis=-1, keepdims=True) + 1e-05)
    normed_part = (row_values * inv_rms * norm_gain.astype(jnp.float32)[None, :]).astype(
        jnp.bfloat16
    )
    rows_per_sec = normed_part.shape[0]
    feature_width = normed_part.shape[1] // n_ten
    normed_rows = lax.dynamic_slice_in_dim(
        normed_part, lax.axis_index("tensor") * feature_width, feature_width, 1
    )
    normed = lax.all_gather(normed_part, "section", axis=0, tiled=True)
    logits = jnp.dot(normed, out_weight, preferred_element_type=jnp.float32)
    shard_width = out_weight.shape[1]
    offset = (lax.axis_index("section") * n_ten + lax.axis_index("tensor")) * shard_width
    columns = offset + lax.iota(jnp.int32, shard_width)
    target_hits = (targets[:, None] == columns[None, :]).astype(jnp.float32)
    own_target = jnp.sum(logits * target_hits, axis=1)
    local_peak = jnp.max(logits, axis=1)
    local_total = jnp.sum(jnp.exp(logits - local_peak[:, None]), axis=1)
    with jax.named_scope("softmax_stats_exchange"):
        stats = exchange_stats(jnp.stack([local_peak, local_total, own_target]))
    row_peak, row_total, target_logit = stats[0], stats[1], stats[2]
    token_loss = row_peak + jnp.log(row_total) - target_logit
    weights = jnp.exp(logits - row_peak[:, None])
    shares = weights / row_total[:, None]
    probs = shares.astype(jnp.bfloat16)
    grad_logits = (shares - target_hits).astype(jnp.bfloat16)
    grad_weight = lax.dot_general(
        normed, probs, (((0,), (0,)), ((), ())), preferred_element_type=jnp.float32
    ).astype(jnp.bfloat16)
    grad_term = lax.dot_general(
        grad_logits, out_weight, (((1,), (1,)), ((), ())), preferred_element_type=jnp.float32
    )
    blocks = grad_term.reshape(n_sec, rows_per_sec, n_ten, feature_width).transpose(0, 2, 1, 3)
    with jax.named_scope("grad_rows_reduce_scatter"):
        grad_normed, (grad_weight, normed_rows, token_loss) = reduce_scatter_blocks(
            blocks, (grad_weight, normed_rows, token_loss)
        )
    return (token_loss, grad_normed.astype(jnp.bfloat16), grad_weight, normed_rows)


def solution(mesh):
    placed = (P("section", None), P(), P(), P(None, ("section", "tensor")))
    return jax.shard_map(
        local,
        mesh=mesh,
        in_specs=placed,
        out_specs=(
            P(),
            P("section", "tensor"),
            P(None, ("section", "tensor")),
            P("section", "tensor"),
        ),
        check_vma=False,
    )
```
